128 devices in a mesh: pipe: 2 (over core), dp: 16 (over y, x), tensor: 4 (over z).
Axes of the slice: x: 4, y: 4, z: 4, core: 2. Of those that a mesh axis runs over, the one named last changes fastest.
Arguments:
- weights: bfloat16 [2, 8192, 8192], P('pipe', 'tensor', 'dp'), may hold values from -0.0625 to 0.0625
- inputs: bfloat16 [2, 2, 32, 64, 8192], P('pipe', None, 'dp', None, 'tensor'), may hold values from -150 to 150
- cotangent: bfloat16 [2, 32, 64, 8192], P(None, 'dp', None, 'tensor'), may hold values from -6 to 6
- clip_norm: float32 [1], replicated, may hold values from 8192 to 12582912
- noise: bfloat16 [2, 8192, 8192], P('pipe', 'tensor', 'dp'), may hold values from -6 to 6
Outputs:
- grads: float32 [2, 8192, 8192], P('pipe', 'tensor', 'dp')
- clip_factors: float32 [2, 32], P(None, 'dp')
The draws below stay inside these ranges and needn't reach their ends.
All inputs are finite; a program needn't handle non-finite values.
Results may differ from the reference program's by a relative error of at most 0.015.
Values may be sent and summed in bfloat16 or wider, within the bound.
No kernel may reach another device: no remote copies, remote signals or barrier semaphores. Data moves between devices by JAX's collectives and lax.ppermute only.
A program may use at most 128 MiB of HBM per device.

```python
import math
import jax
import jax.numpy as jnp
from jax import lax

D = 8192
L = 64
MICRO = 2
SECTIONS = 2
EXAMPLES = 32
N_DP = 16


def draw_inputs(key, part):
    keys = jax.random.split(key, 3)
    base = jnp.clip(jax.random.normal(keys[0], (SECTIONS, MICRO, EXAMPLES, L, D), jnp.float32), -4.0, 4.0)
    position = jnp.arange(D, dtype=jnp.float32) / D
    trend = 0.4 * jnp.exp(math.log(6.0) * position)
    example_scale = jnp.exp(jax.random.uniform(keys[1], (1, MICRO, EXAMPLES, 1, 1), jnp.float32, 0.0, math.log(10.0)))
    rough = jnp.exp(jax.random.uniform(keys[2], (SECTIONS, 1, 1, 1, D), jnp.float32, math.log(0.6), math.log(1.6)))
    values = base * example_scale * rough * trend
    return jnp.clip(values, -150.0, 150.0).astype(jnp.bfloat16)


def draw_clip_norm(key, part):
    factor = jax.random.uniform(key, (1,), jnp.float32, 0.8, 1.2)
    return factor * (4.2 * math.sqrt(L) * D * math.sqrt(2.0 ** SECTIONS - 1.0))


def shard_levels(own_key, dims, shards, smallest, largest):
    level = 1.0
    for dim, blocks in shards:
        draws = jax.random.uniform(jax.random.fold_in(jax.random.fold_in(own_key, 6), dim), (blocks,), jnp.float32, smallest / len(shards), largest / len(shards))
        level = level * jnp.repeat(jnp.exp(draws), dims[dim] // blocks).reshape((-1,) + (1,) * (len(dims) - 1 - dim))
    return level


def scatter_about(rng, dims, spread, reach, cuts=(), kind=jnp.bfloat16):
    entries = spread * jax.random.normal(rng, dims, jnp.float32)
    if cuts:
        entries = entries * shard_levels(rng, dims, cuts, -0.22, 0.18)
    return jnp.clip(entries, -reach, reach).astype(kind)


def setup_inputs(seed: int = 0) -> dict:
    seeds = jax.random.split(jax.random.key(seed), 6)
    weights = scatter_about(seeds[0], (SECTIONS, D, D), D ** -0.5, 0.0625, ((0, 2), (1, 4), (2, 16)))
    inputs = draw_inputs(jax.random.fold_in(seeds[5], 71), 0)
    cotangent = scatter_about(seeds[2], (MICRO, EXAMPLES, L, D), 1.0, 6.0, ((1, 16), (3, 4)))
    clip_norm = draw_clip_norm(jax.random.fold_in(seeds[5], 71), 0)
    noise = scatter_about(seeds[4], (SECTIONS, D, D), 1.0, 6.0, ((0, 2), (1, 4), (2, 16)))
    return dict(weights=weights, inputs=inputs, cotangent=cotangent, clip_norm=clip_norm, noise=noise)


def section_backward(incoming_gradient, weight_matrix):
    flat = incoming_gradient.reshape(-1, D)
    width_block = D // N_DP
    summed = jnp.zeros(flat.shape, jnp.float32)
    for block_index in range(N_DP):
        low = block_index * width_block
        partial_term = jnp.dot(flat[:, low:low + width_block], weight_matrix[:, low:low + width_block].T, preferred_element_type=jnp.float32)
        rounded = lax.optimization_barrier(partial_term.astype(jnp.bfloat16))
        summed = summed + rounded.astype(jnp.float32)
    renewed = flat.astype(jnp.float32) + summed
    return renewed.astype(jnp.bfloat16).reshape(incoming_gradient.shape)

def token_grams(values):
    wide = values.astype(jnp.float32)
    return jnp.einsum('...ld,...kd->...lk', wide, wide)

def reference(weights, inputs, cotangent, clip_norm, noise):
    incoming_gradient = cotangent
    output_grads = [None] * SECTIONS
    for section_index in range(SECTIONS - 1, -1, -1):
        output_grads[section_index] = incoming_gradient
        if section_index > 0:
            incoming_gradient = section_backward(incoming_gradient, weights[section_index])
    norm_square = jnp.zeros((MICRO, EXAMPLES), jnp.float32)
    for section_index in range(SECTIONS):
        input_gram = token_grams(inputs[section_index])
        grad_gram = token_grams(output_grads[section_index])
        norm_square = norm_square + lax.optimization_barrier(jnp.sum(input_gram * grad_gram, axis=(2, 3)))
    bound = clip_norm[0]
    scale_terms = bound / jnp.maximum(jnp.sqrt(norm_square), bound)
    noise_weight = 1.5 / D
    results = []
    for section_index in range(SECTIONS):
        clipped = (inputs[section_index].astype(jnp.float32) * scale_terms[:, :, None, None]).astype(jnp.bfloat16)
        summed = jnp.dot(clipped.reshape(-1, D).T, output_grads[section_index].reshape(-1, D), preferred_element_type=jnp.float32)
        results.append((summed + noise_weight * bound * noise[section_index].astype(jnp.float32)) / (MICRO * EXAMPLES))
    return (jnp.stack(results), scale_terms)
```

```python
import jax
import jax.numpy as jnp
from jax import lax
from jax.sharding import PartitionSpec as P


def swapped(value, axis):
    count = lax.axis_size(axis)
    return lax.ppermute(value, axis, [(source, count - 1 - source) for source in range(count)])


def to_column_blocks(values, group_count, column_part):
    micro_count, example_count, length_count, _ = values.shape
    token_count = example_count * length_count
    full = lax.all_gather(values, "tensor", axis=3, tiled=True)
    by_block = full.reshape(micro_count, token_count, group_count, column_part)
    moved = lax.all_to_all(by_block, "dp", split_axis=2, concat_axis=1, tiled=True)
    return moved.reshape(micro_count, group_count * token_count, column_part)


def grams(values):
    return lax.psum(
        jnp.einsum("...ld,...kd->...lk", values, values, preferred_element_type=jnp.float32), "tensor"
    )


def local(weights, inputs, cotangent, clip_norm, noise):
    section_index = lax.axis_index("pipe")
    group_count = lax.axis_size("dp")
    weight_block = weights[0]
    local_inputs = inputs[0]
    micro_count, example_count, length_count, width_part = local_inputs.shape
    token_count = example_count * length_count
    column_part = weight_block.shape[1]
    full_width = column_part * group_count
    is_last = section_index == 1

    gathered_inputs = lax.all_gather(local_inputs, "dp", axis=1, tiled=True)
    input_grams = grams(local_inputs)
    last_grams = grams(cotangent)
    last_blocks = to_column_blocks(cotangent, group_count, column_part)

    last_weights = jnp.where(is_last, weight_block, swapped(weight_block, "pipe"))
    own_blocks = lax.dynamic_index_in_dim(last_blocks, section_index, 0, keepdims=False)
    own_cotangent = lax.dynamic_index_in_dim(cotangent, section_index, 0, keepdims=False)
    terms = lax.dot_general(
        own_blocks, last_weights, (((1,), (1,)), ((), ())), preferred_element_type=jnp.float32
    ).astype(jnp.bfloat16)
    summed = lax.psum_scatter(terms, "dp", scatter_dimension=0, tiled=True).astype(jnp.float32)
    renewed = (own_cotangent.reshape(token_count, width_part).astype(jnp.float32) + summed).astype(
        jnp.bfloat16
    ).reshape(1, example_count, length_count, width_part)

    own_first_grams = grams(renewed)
    other_first_grams = swapped(own_first_grams, "pipe")
    first_grams = jnp.where(
        is_last,
        jnp.concatenate([other_first_grams, own_first_grams], 0),
        jnp.concatenate([own_first_grams, other_first_grams], 0),
    )
    output_grams = jnp.where(is_last, last_grams, first_grams)
    section_terms = jnp.sum(input_grams * output_grams, axis=(2, 3))
    norm_square = lax.psum(section_terms, "pipe")
    bound = clip_norm[0]
    scale_terms = bound / jnp.maximum(jnp.sqrt(norm_square), bound)
    all_scales = lax.all_gather(scale_terms, "dp", axis=1, tiled=True)

    own_first_blocks = to_column_blocks(renewed, group_count, column_part)
    other_first_blocks = swapped(own_first_blocks, "pipe")
    first_blocks = jnp.where(
        is_last,
        jnp.concatenate([other_first_blocks, own_first_blocks], 0),
        jnp.concatenate([own_first_blocks, other_first_blocks], 0),
    )
    grad_blocks = jnp.where(is_last, last_blocks, first_blocks)

    clipped = (gathered_inputs.astype(jnp.float32) * all_scales[:, :, None, None]).astype(jnp.bfloat16)
    flat_inputs = clipped.reshape(micro_count * group_count * token_count, width_part)
    flat_grads = grad_blocks.reshape(micro_count * group_count * token_count, column_part)
    summed_grad = lax.dot_general(
        flat_inputs, flat_grads, (((0,), (0,)), ((), ())), preferred_element_type=jnp.float32
    )
    noise_weight = 1.5 / full_width
    per_example_sum = micro_count * group_count * example_count
    final_output = (
        summed_grad + noise_weight * bound * noise[0].astype(jnp.float32)
    ) / per_example_sum
    return (final_output[None], scale_terms)


def solution(mesh):
    in_specs = (
        P("pipe", "tensor", "dp"),
        P("pipe", None, "dp", None, "tensor"),
        P(None, "dp", None, "tensor"),
        P(),
        P("pipe", "tensor", "dp"),
    )
    out_specs = (P("pipe", "tensor", "dp"), P(None, "dp"))
    return jax.shard_map(local, mesh=mesh, in_specs=in_specs, out_specs=out_specs, check_vma=False)
```

```python
import jax
import jax.numpy as jnp
from jax import lax
from jax.sharding import PartitionSpec as P


def swapped(value, axis):
    count = lax.axis_size(axis)
    return lax.ppermute(value, axis, [(source, count - 1 - source) for source in range(count)])


def gather_features(values, axis):
    count = lax.axis_size(axis)
    position = lax.axis_index(axis)
    pieces = [values]
    for offset in range(1, count):
        pieces.append(
            lax.ppermute(values, axis, [(source, (source + offset) % count) for source in range(count)])
        )
    stacked = jnp.stack(pieces)
    order = (position - jnp.arange(count)) % count
    ordered = jnp.take(stacked, order, axis=0)
    ordered = jnp.moveaxis(ordered, 0, -2)
    return ordered.reshape(values.shape[:-1] + (count * values.shape[-1],))


def to_column_blocks(full, group_count, column_part):
    example_count, length_count, _ = full.shape
    token_count = example_count * length_count
    by_block = full.reshape(token_count, group_count, column_part)
    moved = lax.all_to_all(by_block, "dp", split_axis=1, concat_axis=0, tiled=True)
    return moved.reshape(group_count * token_count, column_part)


def token_grams(values):
    return jnp.einsum("...ld,...kd->...lk", values, values, preferred_element_type=jnp.float32)


def by_micro(is_last, own, other):
    return jnp.where(is_last, jnp.stack([other, own]), jnp.stack([own, other]))


def local(weights, inputs, cotangent, clip_norm, noise):
    section_index = lax.axis_index("pipe")
    group_count = lax.axis_size("dp")
    weight_block = weights[0]
    local_inputs = inputs[0]
    micro_count, example_count, length_count, width_part = local_inputs.shape
    token_count = example_count * length_count
    column_part = weight_block.shape[1]
    full_width = column_part * group_count
    is_last = section_index == 1

    gathered_inputs = lax.all_gather(local_inputs, "dp", axis=1, tiled=True)
    input_grams = lax.psum(token_grams(local_inputs), "tensor")
    other_input_grams = swapped(input_grams, "pipe")

    own_cotangent = lax.dynamic_index_in_dim(cotangent, section_index, 0, keepdims=False)
    full_last = gather_features(own_cotangent, "tensor")
    last_grams = token_grams(full_last)
    last_blocks = to_column_blocks(full_last, group_count, column_part)
    last_blocks_other = swapped(last_blocks, "pipe")

    last_weights = jnp.where(is_last, weight_block, swapped(weight_block, "pipe"))
    terms = lax.dot_general(
        last_blocks, last_weights, (((1,), (1,)), ((), ())), preferred_element_type=jnp.float32
    ).astype(jnp.bfloat16)
    summed = lax.psum_scatter(terms, "dp", scatter_dimension=0, tiled=True).astype(jnp.float32)
    renewed = (own_cotangent.reshape(token_count, width_part).astype(jnp.float32) + summed).astype(
        jnp.bfloat16
    ).reshape(example_count, length_count, width_part)
    full_first = gather_features(renewed, "tensor")
    first_grams = token_grams(full_first)
    first_blocks = to_column_blocks(full_first, group_count, column_part)
    first_blocks_other = swapped(first_blocks, "pipe")

    own_input_grams = lax.dynamic_index_in_dim(input_grams, section_index, 0, keepdims=False)
    held_input_grams = lax.dynamic_index_in_dim(other_input_grams, section_index, 0, keepdims=False)
    last_input_grams = jnp.where(is_last, own_input_grams, held_input_grams)
    first_input_grams = jnp.where(is_last, held_input_grams, own_input_grams)
    norm_square = jnp.sum(first_input_grams * first_grams, axis=(1, 2)) + jnp.sum(
        last_input_grams * last_grams, axis=(1, 2)
    )
    bound = clip_norm[0]
    own_scales = bound / jnp.maximum(jnp.sqrt(norm_square), bound)
    scale_terms = by_micro(is_last, own_scales, swapped(own_scales, "pipe"))
    all_scales = lax.all_gather(scale_terms, "dp", axis=1, tiled=True)

    grad_blocks = jnp.where(
        is_last,
        by_micro(is_last, last_blocks, last_blocks_other),
        by_micro(is_last, first_blocks, first_blocks_other),
    )
    clipped = (gathered_inputs.astype(jnp.float32) * all_scales[:, :, None, None]).astype(jnp.bfloat16)
    flat_inputs = clipped.reshape(micro_count * group_count * token_count, width_part)
    flat_grads = grad_blocks.reshape(micro_count * group_count * token_count, column_part)
    summed_grad = lax.dot_general(
        flat_inputs, flat_grads, (((0,), (0,)), ((), ())), preferred_element_type=jnp.float32
    )
    noise_weight = 1.5 / full_width
    per_example_sum = micro_count * group_count * example_count
    final_output = (
        summed_grad + noise_weight * bound * noise[0].astype(jnp.float32)
    ) / per_example_sum
    return (final_output[None], scale_terms)


def solution(mesh):
    in_specs = (
        P("pipe", "tensor", "dp"),
        P("pipe", None, "dp", None, "tensor"),
        P(None, "dp", None, "tensor"),
        P(),
        P("pipe", "tensor", "dp"),
    )
    out_specs = (P("pipe", "tensor", "dp"), P(None, "dp"))
    return jax.shard_map(local, mesh=mesh, in_specs=in_specs, out_specs=out_specs, check_vma=False)
```

```python
import jax
import jax.numpy as jnp
from jax import lax
from jax.sharding import PartitionSpec as P


def swapped(value, axis):
    count = lax.axis_size(axis)
    return lax.ppermute(value, axis, [(source, count - 1 - source) for source in range(count)])


def ring_pieces(values, axis):
    count = lax.axis_size(axis)
    position = lax.axis_index(axis)
    pieces = [values]
    for offset in range(1, count):
        pieces.append(
            lax.ppermute(values, axis, [(source, (source + offset) % count) for source in range(count)])
        )
    stacked = jnp.stack(pieces)
    return stacked, (position - jnp.arange(count)) % count


def column_blocks(values, group_count, column_part):
    example_count, length_count, width_part = values.shape
    token_count = example_count * length_count
    stacked, order = ring_pieces(values, "tensor")
    grams = jnp.einsum("jeld,jekd->elk", stacked, stacked, preferred_element_type=jnp.float32)
    pieces = stacked.shape[0]
    per_piece = width_part // column_part
    chunks = stacked.reshape(pieces, token_count, per_piece, column_part).transpose(0, 2, 1, 3)
    chunks = jnp.take(chunks, order, axis=0).reshape(pieces * per_piece, token_count, column_part)
    moved = lax.all_to_all(chunks, "dp", split_axis=0, concat_axis=1, tiled=True)
    return grams, moved.reshape(group_count * token_count, column_part)


def token_grams(values):
    return jnp.einsum("...ld,...kd->...lk", values, values, preferred_element_type=jnp.float32)


def by_micro(is_last, own, other):
    return jnp.where(is_last, jnp.stack([other, own]), jnp.stack([own, other]))


def local(weights, inputs, cotangent, clip_norm, noise):
    section_index = lax.axis_index("pipe")
    group_count = lax.axis_size("dp")
    weight_block = weights[0]
    local_inputs = inputs[0]
    micro_count, example_count, length_count, width_part = local_inputs.shape
    token_count = example_count * length_count
    column_part = weight_block.shape[1]
    full_width = column_part * group_count
    is_last = section_index == 1

    gathered_inputs = lax.all_gather(local_inputs, "dp", axis=1, tiled=True)
    input_grams = lax.psum(token_grams(local_inputs), "tensor")
    other_input_grams = swapped(input_grams, "pipe")

    own_cotangent = lax.dynamic_index_in_dim(cotangent, section_index, 0, keepdims=False)
    last_grams, last_blocks = column_blocks(own_cotangent, group_count, column_part)
    last_blocks_other = swapped(last_blocks, "pipe")

    last_weights = jnp.where(is_last, weight_block, swapped(weight_block, "pipe"))
    terms = lax.dot_general(
        last_blocks, last_weights, (((1,), (1,)), ((), ())), preferred_element_type=jnp.float32
    ).astype(jnp.bfloat16)
    summed = lax.psum_scatter(terms, "dp", scatter_dimension=0, tiled=True).astype(jnp.float32)
    renewed = (own_cotangent.reshape(token_count, width_part).astype(jnp.float32) + summed).astype(
        jnp.bfloat16
    ).reshape(example_count, length_count, width_part)
    first_grams, first_blocks = column_blocks(renewed, group_count, column_part)
    first_blocks_other = swapped(first_blocks, "pipe")

    own_input_grams = lax.dynamic_index_in_dim(input_grams, section_index, 0, keepdims=False)
    held_input_grams = lax.dynamic_index_in_dim(other_input_grams, section_index, 0, keepdims=False)
    last_input_grams = jnp.where(is_last, own_input_grams, held_input_grams)
    first_input_grams = jnp.where(is_last, held_input_grams, own_input_grams)
    norm_square = jnp.sum(first_input_grams * first_grams, axis=(1, 2)) + jnp.sum(
        last_input_grams * last_grams, axis=(1, 2)
    )
    bound = clip_norm[0]
    own_scales = bound / jnp.maximum(jnp.sqrt(norm_square), bound)
    scale_terms = by_micro(is_last, own_scales, swapped(own_scales, "pipe"))
    scale_pieces, scale_order = ring_pieces(scale_terms, "dp")
    all_scales = jnp.take(scale_pieces, scale_order, axis=0).transpose(1, 0, 2)

    grad_blocks = jnp.where(
        is_last,
        by_micro(is_last, last_blocks, last_blocks_other),
        by_micro(is_last, first_blocks, first_blocks_other),
    )
    scaled_blocks = (
        grad_blocks.reshape(micro_count, group_count, example_count, length_count, column_part).astype(
            jnp.float32
        )
        * all_scales[:, :, :, None, None]
    ).astype(jnp.bfloat16)
    flat_inputs = gathered_inputs.reshape(micro_count * group_count * token_count, width_part)
    flat_grads = scaled_blocks.reshape(micro_count * group_count * token_count, column_part)
    summed_grad = lax.dot_general(
        flat_inputs, flat_grads, (((0,), (0,)), ((), ())), preferred_element_type=jnp.float32
    )
    noise_weight = 1.5 / full_width
    per_example_sum = micro_count * group_count * example_count
    final_output = (
        summed_grad + noise_weight * bound * noise[0].astype(jnp.float32)
    ) / per_example_sum
    return (final_output[None], scale_terms)


def solution(mesh):
    in_specs = (
        P("pipe", "tensor", "dp"),
        P("pipe", None, "dp", None, "tensor"),
        P(None, "dp", None, "tensor"),
        P(),
        P("pipe", "tensor", "dp"),
    )
    out_specs = (P("pipe", "tensor", "dp"), P(None, "dp"))
    return jax.shard_map(local, mesh=mesh, in_specs=in_specs, out_specs=out_specs, check_vma=False)
```

```python
import jax
import jax.numpy as jnp
from jax import lax
from jax.sharding import PartitionSpec as P


def swapped(value, axis):
    count = lax.axis_size(axis)
    return lax.ppermute(value, axis, [(source, count - 1 - source) for source in range(count)])


def ring_pieces(values, axis):
    count = lax.axis_size(axis)
    position = lax.axis_index(axis)
    pieces = [values]
    for offset in range(1, count):
        pieces.append(
            lax.ppermute(values, axis, [(source, (source + offset) % count) for source in range(count)])
        )
    stacked = jnp.stack(pieces)
    return stacked, (position - jnp.arange(count)) % count


def feature_pieces(values):
    stacked, order = ring_pieces(values, "tensor")
    grams = jnp.einsum("jeld,jekd->elk", stacked, stacked, preferred_element_type=jnp.float32)
    return stacked, order, grams


def column_blocks(stacked, order, group_count, column_part, row_scales=None):
    pieces, example_count, length_count, width_part = stacked.shape
    token_count = example_count * length_count
    if row_scales is not None:
        stacked = (stacked.astype(jnp.float32) * row_scales[None, :, None, None]).astype(jnp.bfloat16)
    per_piece = width_part // column_part
    chunks = stacked.reshape(pieces, token_count, per_piece, column_part).transpose(0, 2, 1, 3)
    chunks = jnp.take(chunks, order, axis=0).reshape(pieces * per_piece, token_count, column_part)
    moved = lax.all_to_all(chunks, "dp", split_axis=0, concat_axis=1, tiled=True)
    return moved.reshape(group_count * token_count, column_part)


def token_grams(values):
    return jnp.einsum("...ld,...kd->...lk", values, values, preferred_element_type=jnp.float32)


def by_micro(is_last, own, other):
    return jnp.where(is_last, jnp.stack([other, own]), jnp.stack([own, other]))


def local(weights, inputs, cotangent, clip_norm, noise):
    section_index = lax.axis_index("pipe")
    group_count = lax.axis_size("dp")
    weight_block = weights[0]
    local_inputs = inputs[0]
    micro_count, example_count, length_count, width_part = local_inputs.shape
    token_count = example_count * length_count
    column_part = weight_block.shape[1]
    full_width = column_part * group_count
    is_last = section_index == 1

    gathered_inputs = lax.all_gather(local_inputs, "dp", axis=1, tiled=True)
    input_grams = lax.psum(token_grams(local_inputs), "tensor")
    other_input_grams = swapped(input_grams, "pipe")

    own_cotangent = lax.dynamic_index_in_dim(cotangent, section_index, 0, keepdims=False)
    last_pieces, last_order, last_grams = feature_pieces(own_cotangent)
    last_blocks = column_blocks(last_pieces, last_order, group_count, column_part)
    last_blocks_other = swapped(last_blocks, "pipe")

    last_weights = jnp.where(is_last, weight_block, swapped(weight_block, "pipe"))
    terms = lax.dot_general(
        last_blocks, last_weights, (((1,), (1,)), ((), ())), preferred_element_type=jnp.float32
    ).astype(jnp.bfloat16)
    summed = lax.psum_scatter(terms, "dp", scatter_dimension=0, tiled=True).astype(jnp.float32)
    renewed = (own_cotangent.reshape(token_count, width_part).astype(jnp.float32) + summed).astype(
        jnp.bfloat16
    ).reshape(example_count, length_count, width_part)
    first_pieces, first_order, first_grams = feature_pieces(renewed)

    own_input_grams = lax.dynamic_index_in_dim(input_grams, section_index, 0, keepdims=False)
    held_input_grams = lax.dynamic_index_in_dim(other_input_grams, section_index, 0, keepdims=False)
    last_input_grams = jnp.where(is_last, own_input_grams, held_input_grams)
    first_input_grams = jnp.where(is_last, held_input_grams, own_input_grams)
    norm_square = jnp.sum(first_input_grams * first_grams, axis=(1, 2)) + jnp.sum(
        last_input_grams * last_grams, axis=(1, 2)
    )
    bound = clip_norm[0]
    own_scales = bound / jnp.maximum(jnp.sqrt(norm_square), bound)
    scale_terms = by_micro(is_last, own_scales, swapped(own_scales, "pipe"))
    all_scales = lax.all_gather(scale_terms, "dp", axis=1, tiled=True)

    first_blocks = column_blocks(first_pieces, first_order, group_count, column_part, own_scales)
    first_blocks_other = swapped(first_blocks, "pipe")

    grad_blocks = jnp.where(
        is_last,
        by_micro(is_last, last_blocks, last_blocks_other),
        by_micro(is_last, first_blocks, first_blocks_other),
    )
    row_scales = jnp.where(is_last, all_scales, jnp.ones_like(all_scales))
    scaled_blocks = (
        grad_blocks.reshape(micro_count, group_count, example_count, length_count, column_part).astype(
            jnp.float32
        )
        * row_scales.reshape(micro_count, group_count, example_count)[:, :, :, None, None]
    ).astype(jnp.bfloat16)
    flat_inputs = gathered_inputs.reshape(micro_count * group_count * token_count, width_part)
    flat_grads = scaled_blocks.reshape(micro_count * group_count * token_count, column_part)
    summed_grad = lax.dot_general(
        flat_inputs, flat_grads, (((0,), (0,)), ((), ())), preferred_element_type=jnp.float32
    )
    noise_weight = 1.5 / full_width
    per_example_sum = micro_count * group_count * example_count
    final_output = (
        summed_grad + noise_weight * bound * noise[0].astype(jnp.float32)
    ) / per_example_sum
    return (final_output[None], scale_terms)


def solution(mesh):
    in_specs = (
        P("pipe", "tensor", "dp"),
        P("pipe", None, "dp", None, "tensor"),
        P(None, "dp", None, "tensor"),
        P(),
        P("pipe", "tensor", "dp"),
    )
    out_specs = (P("pipe", "tensor", "dp"), P(None, "dp"))
    return jax.shard_map(local, mesh=mesh, in_specs=in_specs, out_specs=out_specs, check_vma=False)
```

```python
import jax
import jax.numpy as jnp
from jax import lax
from jax.sharding import PartitionSpec as P


def swapped(value, axis):
    count = lax.axis_size(axis)
    return lax.ppermute(value, axis, [(source, count - 1 - source) for source in range(count)])


def ring_pieces(values, axis):
    count = lax.axis_size(axis)
    position = lax.axis_index(axis)
    pieces = [values]
    for offset in range(1, count):
        pieces.append(
            lax.ppermute(values, axis, [(source, (source + offset) % count) for source in range(count)])
        )
    stacked = jnp.stack(pieces)
    return stacked, (position - jnp.arange(count)) % count


def feature_pieces(values):
    stacked, order = ring_pieces(values, "tensor")
    grams = jnp.einsum("jeld,jekd->elk", stacked, stacked, preferred_element_type=jnp.float32)
    return stacked, order, grams


def column_blocks(stacked, order, group_count, column_part, row_scales=None):
    pieces, example_count, length_count, width_part = stacked.shape
    token_count = example_count * length_count
    if row_scales is not None:
        stacked = (stacked.astype(jnp.float32) * row_scales[None, :, None, None]).astype(jnp.bfloat16)
    per_piece = width_part // column_part
    chunks = stacked.reshape(pieces, token_count, per_piece, column_part).transpose(0, 2, 1, 3)
    chunks = jnp.take(chunks, order, axis=0).reshape(pieces * per_piece, token_count, column_part)
    moved = lax.all_to_all(chunks, "dp", split_axis=0, concat_axis=1, tiled=True)
    return moved.reshape(group_count * token_count, column_part)


def token_grams(values):
    return jnp.einsum("...ld,...kd->...lk", values, values, preferred_element_type=jnp.float32)


def by_micro(is_last, own, other):
    return jnp.where(is_last, jnp.stack([other, own]), jnp.stack([own, other]))


def local(weights, inputs, cotangent, clip_norm, noise):
    section_index = lax.axis_index("pipe")
    group_count = lax.axis_size("dp")
    weight_block = weights[0]
    local_inputs = inputs[0]
    micro_count, example_count, length_count, width_part = local_inputs.shape
    token_count = example_count * length_count
    column_part = weight_block.shape[1]
    full_width = column_part * group_count
    is_last = section_index == 1

    gathered_inputs = jnp.concatenate(
        [lax.all_gather(local_inputs[m : m + 1], "dp", axis=1, tiled=True) for m in range(micro_count)], axis=0
    )
    input_grams = lax.psum(token_grams(local_inputs), "tensor")
    other_input_grams = swapped(input_grams, "pipe")

    own_cotangent = lax.dynamic_index_in_dim(cotangent, section_index, 0, keepdims=False)
    last_pieces, last_order, last_grams = feature_pieces(own_cotangent)
    last_blocks = column_blocks(last_pieces, last_order, group_count, column_part)
    last_blocks_other = swapped(last_blocks, "pipe")

    last_weights = jnp.where(is_last, weight_block, swapped(weight_block, "pipe"))
    terms = lax.dot_general(
        last_blocks, last_weights, (((1,), (1,)), ((), ())), preferred_element_type=jnp.float32
    ).astype(jnp.bfloat16)
    halves = jnp.split(terms, 2, axis=1)
    summed = jnp.concatenate(
        [lax.psum_scatter(half, "dp", scatter_dimension=0, tiled=True) for half in halves], axis=1
    ).astype(jnp.float32)
    renewed = (own_cotangent.reshape(token_count, width_part).astype(jnp.float32) + summed).astype(
        jnp.bfloat16
    ).reshape(example_count, length_count, width_part)
    first_pieces, first_order, first_grams = feature_pieces(renewed)

    own_input_grams = lax.dynamic_index_in_dim(input_grams, section_index, 0, keepdims=False)
    held_input_grams = lax.dynamic_index_in_dim(other_input_grams, section_index, 0, keepdims=False)
    last_input_grams = jnp.where(is_last, own_input_grams, held_input_grams)
    first_input_grams = jnp.where(is_last, held_input_grams, own_input_grams)
    norm_square = jnp.sum(first_input_grams * first_grams, axis=(1, 2)) + jnp.sum(
        last_input_grams * last_grams, axis=(1, 2)
    )
    bound = clip_norm[0]
    own_scales = bound / jnp.maximum(jnp.sqrt(norm_square), bound)
    scale_terms = by_micro(is_last, own_scales, swapped(own_scales, "pipe"))
    all_scales = lax.all_gather(scale_terms, "dp", axis=1, tiled=True)

    first_blocks = column_blocks(first_pieces, first_order, group_count, column_part, own_scales)
    first_blocks_other = swapped(first_blocks, "pipe")

    grad_blocks = jnp.where(
        is_last,
        by_micro(is_last, last_blocks, last_blocks_other),
        by_micro(is_last, first_blocks, first_blocks_other),
    )
    row_scales = jnp.where(is_last, all_scales, jnp.ones_like(all_scales))
    scaled_blocks = (
        grad_blocks.reshape(micro_count, group_count, example_count, length_count, column_part).astype(
            jnp.float32
        )
        * row_scales.reshape(micro_count, group_count, example_count)[:, :, :, None, None]
    ).astype(jnp.bfloat16)
    flat_inputs = gathered_inputs.reshape(micro_count * group_count * token_count, width_part)
    flat_grads = scaled_blocks.reshape(micro_count * group_count * token_count, column_part)
    summed_grad = lax.dot_general(
        flat_inputs, flat_grads, (((0,), (0,)), ((), ())), preferred_element_type=jnp.float32
    )
    noise_weight = 1.5 / full_width
    per_example_sum = micro_count * group_count * example_count
    final_output = (
        summed_grad + noise_weight * bound * noise[0].astype(jnp.float32)
    ) / per_example_sum
    return (final_output[None], scale_terms)


def solution(mesh):
    in_specs = (
        P("pipe", "tensor", "dp"),
        P("pipe", None, "dp", None, "tensor"),
        P(None, "dp", None, "tensor"),
        P(),
        P("pipe", "tensor", "dp"),
    )
    out_specs = (P("pipe", "tensor", "dp"), P(None, "dp"))
    return jax.shard_map(local, mesh=mesh, in_specs=in_specs, out_specs=out_specs, check_vma=False)
```

```python
import jax
import jax.numpy as jnp
from jax import lax
from jax.sharding import PartitionSpec as P


def swapped(value, axis):
    count = lax.axis_size(axis)
    return lax.ppermute(value, axis, [(source, count - 1 - source) for source in range(count)])


def ring_pieces(values, axis):
    count = lax.axis_size(axis)
    position = lax.axis_index(axis)
    pieces = [values]
    for offset in range(1, count):
        pieces.append(
            lax.ppermute(values, axis, [(source, (source + offset) % count) for source in range(count)])
        )
    stacked = jnp.stack(pieces)
    return stacked, (position - jnp.arange(count)) % count


def feature_pieces(values):
    stacked, order = ring_pieces(values, "tensor")
    grams = jnp.einsum("jeld,jekd->elk", stacked, stacked, preferred_element_type=jnp.float32)
    return stacked, order, grams


def column_blocks(stacked, order, group_count, column_part, row_scales=None):
    pieces, example_count, length_count, width_part = stacked.shape
    token_count = example_count * length_count
    if row_scales is not None:
        stacked = (stacked.astype(jnp.float32) * row_scales[None, :, None, None]).astype(jnp.bfloat16)
    per_piece = width_part // column_part
    chunks = stacked.reshape(pieces, token_count, per_piece, column_part).transpose(0, 2, 1, 3)
    chunks = jnp.take(chunks, order, axis=0).reshape(pieces * per_piece, token_count, column_part)
    extra = 0
    if row_scales is not None:
        parts = []
        rest = row_scales
        for _ in range(3):
            part = rest.astype(jnp.bfloat16)
            parts.append(part)
            rest = rest - part.astype(jnp.float32)
        extra = 16
        rows = jnp.zeros((extra, column_part), jnp.bfloat16)
        rows = rows.at[: len(parts), :example_count].set(jnp.stack(parts))
        rows = jnp.broadcast_to(rows[None], (pieces * per_piece, extra, column_part))
        chunks = jnp.concatenate([chunks, rows], axis=1)
    moved = lax.all_to_all(chunks, "dp", split_axis=0, concat_axis=1, tiled=True)
    moved = moved.reshape(group_count, token_count + extra, column_part)
    blocks = moved[:, :token_count].reshape(group_count * token_count, column_part)
    if row_scales is None:
        return blocks
    received = moved[:, token_count : token_count + 3, :example_count].astype(jnp.float32)
    return blocks, (received[:, 2] + received[:, 1]) + received[:, 0]


def token_grams(values):
    return jnp.einsum("...ld,...kd->...lk", values, values, preferred_element_type=jnp.float32)


def by_micro(is_last, own, other):
    return jnp.where(is_last, jnp.stack([other, own]), jnp.stack([own, other]))


def local(weights, inputs, cotangent, clip_norm, noise):
    section_index = lax.axis_index("pipe")
    group_count = lax.axis_size("dp")
    weight_block = weights[0]
    local_inputs = inputs[0]
    micro_count, example_count, length_count, width_part = local_inputs.shape
    token_count = example_count * length_count
    column_part = weight_block.shape[1]
    full_width = column_part * group_count
    is_last = section_index == 1

    gathered_inputs = lax.all_gather(local_inputs, "dp", axis=1, tiled=True)
    input_grams = lax.psum(token_grams(local_inputs), "tensor")
    other_input_grams = swapped(input_grams, "pipe")

    own_cotangent = lax.dynamic_index_in_dim(cotangent, section_index, 0, keepdims=False)
    last_pieces, last_order, last_grams = feature_pieces(own_cotangent)
    last_blocks = column_blocks(last_pieces, last_order, group_count, column_part)
    last_blocks_other = swapped(last_blocks, "pipe")

    last_weights = jnp.where(is_last, weight_block, swapped(weight_block, "pipe"))
    terms = lax.dot_general(
        last_blocks, last_weights, (((1,), (1,)), ((), ())), preferred_element_type=jnp.float32
    ).astype(jnp.bfloat16)
    summed = lax.psum_scatter(terms, "dp", scatter_dimension=0, tiled=True).astype(jnp.float32)
    renewed = (own_cotangent.reshape(token_count, width_part).astype(jnp.float32) + summed).astype(
        jnp.bfloat16
    ).reshape(example_count, length_count, width_part)
    first_pieces, first_order, first_grams = feature_pieces(renewed)

    own_input_grams = lax.dynamic_index_in_dim(input_grams, section_index, 0, keepdims=False)
    held_input_grams = lax.dynamic_index_in_dim(other_input_grams, section_index, 0, keepdims=False)
    last_input_grams = jnp.where(is_last, own_input_grams, held_input_grams)
    first_input_grams = jnp.where(is_last, held_input_grams, own_input_grams)
    norm_square = jnp.sum(first_input_grams * first_grams, axis=(1, 2)) + jnp.sum(
        last_input_grams * last_grams, axis=(1, 2)
    )
    bound = clip_norm[0]
    own_scales = bound / jnp.maximum(jnp.sqrt(norm_square), bound)
    scale_terms = by_micro(is_last, own_scales, swapped(own_scales, "pipe"))

    first_blocks, group_scales = column_blocks(first_pieces, first_order, group_count, column_part, own_scales)
    first_blocks_other = swapped(first_blocks, "pipe")
    all_scales = by_micro(is_last, group_scales, swapped(group_scales, "pipe"))

    grad_blocks = jnp.where(
        is_last,
        by_micro(is_last, last_blocks, last_blocks_other),
        by_micro(is_last, first_blocks, first_blocks_other),
    )
    row_scales = jnp.where(is_last, all_scales, jnp.ones_like(all_scales))
    scaled_blocks = (
        grad_blocks.reshape(micro_count, group_count, example_count, length_count, column_part).astype(
            jnp.float32
        )
        * row_scales.reshape(micro_count, group_count, example_count)[:, :, :, None, None]
    ).astype(jnp.bfloat16)
    flat_inputs = gathered_inputs.reshape(micro_count * group_count * token_count, width_part)
    flat_grads = scaled_blocks.reshape(micro_count * group_count * token_count, column_part)
    summed_grad = lax.dot_general(
        flat_inputs, flat_grads, (((0,), (0,)), ((), ())), preferred_element_type=jnp.float32
    )
    noise_weight = 1.5 / full_width
    per_example_sum = micro_count * group_count * example_count
    final_output = (
        summed_grad + noise_weight * bound * noise[0].astype(jnp.float32)
    ) / per_example_sum
    return (final_output[None], scale_terms)


def solution(mesh):
    in_specs = (
        P("pipe", "tensor", "dp"),
        P("pipe", None, "dp", None, "tensor"),
        P(None, "dp", None, "tensor"),
        P(),
        P("pipe", "tensor", "dp"),
    )
    out_specs = (P("pipe", "tensor", "dp"), P(None, "dp"))
    return jax.shard_map(local, mesh=mesh, in_specs=in_specs, out_specs=out_specs, check_vma=False)
```

```python
import jax
import jax.numpy as jnp
from jax import lax
from jax.sharding import PartitionSpec as P


def swapped(value, axis):
    count = lax.axis_size(axis)
    return lax.ppermute(value, axis, [(source, count - 1 - source) for source in range(count)])


def ring_pieces(values, axis):
    count = lax.axis_size(axis)
    position = lax.axis_index(axis)
    pieces = [values]
    for offset in range(1, count):
        pieces.append(
            lax.ppermute(values, axis, [(source, (source + offset) % count) for source in range(count)])
        )
    stacked = jnp.stack(pieces)
    return stacked, (position - jnp.arange(count)) % count


def feature_pieces(values):
    stacked, order = ring_pieces(values, "tensor")
    grams = jnp.einsum("jeld,jekd->elk", stacked, stacked, preferred_element_type=jnp.float32)
    return stacked, order, grams


def column_blocks(stacked, order, group_count, column_part, row_scales=None):
    pieces, example_count, length_count, width_part = stacked.shape
    token_count = example_count * length_count
    if row_scales is not None:
        stacked = (stacked.astype(jnp.float32) * row_scales[None, :, None, None]).astype(jnp.bfloat16)
    per_piece = width_part // column_part
    chunks = stacked.reshape(pieces, token_count, per_piece, column_part).transpose(0, 2, 1, 3)
    chunks = jnp.take(chunks, order, axis=0).reshape(pieces * per_piece, token_count, column_part)
    extra = 0
    if row_scales is not None:
        parts = []
        rest = row_scales
        for _ in range(3):
            part = lax.optimization_barrier(rest.astype(jnp.bfloat16))
            parts.append(part)
            rest = rest - part.astype(jnp.float32)
        extra = 16
        rows = jnp.zeros((extra, column_part), jnp.bfloat16)
        rows = rows.at[: len(parts), :example_count].set(jnp.stack(parts))
        rows = jnp.broadcast_to(rows[None], (pieces * per_piece, extra, column_part))
        chunks = jnp.concatenate([chunks, rows], axis=1)
    moved = lax.all_to_all(chunks, "dp", split_axis=0, concat_axis=1, tiled=True)
    moved = moved.reshape(group_count, token_count + extra, column_part)
    blocks = moved[:, :token_count].reshape(group_count * token_count, column_part)
    if row_scales is None:
        return blocks
    received = moved[:, token_count : token_count + 3, :example_count].astype(jnp.float32)
    return blocks, (received[:, 2] + received[:, 1]) + received[:, 0]


def token_grams(values):
    return jnp.einsum("...ld,...kd->...lk", values, values, preferred_element_type=jnp.float32)


def by_micro(is_last, own, other):
    return jnp.where(is_last, jnp.stack([other, own]), jnp.stack([own, other]))


def local(weights, inputs, cotangent, clip_norm, noise):
    section_index = lax.axis_index("pipe")
    group_count = lax.axis_size("dp")
    weight_block = weights[0]
    local_inputs = inputs[0]
    micro_count, example_count, length_count, width_part = local_inputs.shape
    token_count = example_count * length_count
    column_part = weight_block.shape[1]
    full_width = column_part * group_count
    is_last = section_index == 1

    gathered_inputs = lax.all_gather(local_inputs, "dp", axis=1, tiled=True)
    input_grams = lax.psum(token_grams(local_inputs), "tensor")

    own_cotangent = lax.dynamic_index_in_dim(cotangent, section_index, 0, keepdims=False)
    last_pieces, last_order, last_grams = feature_pieces(own_cotangent)
    last_blocks = column_blocks(last_pieces, last_order, group_count, column_part)
    last_blocks_other = swapped(last_blocks, "pipe")

    last_weights = jnp.where(is_last, weight_block, swapped(weight_block, "pipe"))
    terms = lax.dot_general(
        last_blocks, last_weights, (((1,), (1,)), ((), ())), preferred_element_type=jnp.float32
    ).astype(jnp.bfloat16)
    terms, gathered_inputs, input_grams = lax.optimization_barrier((terms, gathered_inputs, input_grams))
    summed = lax.psum_scatter(terms, "dp", scatter_dimension=0, tiled=True).astype(jnp.float32)
    other_input_grams = swapped(input_grams, "pipe")
    renewed = (own_cotangent.reshape(token_count, width_part).astype(jnp.float32) + summed).astype(
        jnp.bfloat16
    ).reshape(example_count, length_count, width_part)
    first_pieces, first_order, first_grams = feature_pieces(renewed)

    own_input_grams = lax.dynamic_index_in_dim(input_grams, section_index, 0, keepdims=False)
    held_input_grams = lax.dynamic_index_in_dim(other_input_grams, section_index, 0, keepdims=False)
    last_input_grams = jnp.where(is_last, own_input_grams, held_input_grams)
    first_input_grams = jnp.where(is_last, held_input_grams, own_input_grams)
    norm_square = jnp.sum(first_input_grams * first_grams, axis=(1, 2)) + jnp.sum(
        last_input_grams * last_grams, axis=(1, 2)
    )
    bound = clip_norm[0]
    own_scales = bound / jnp.maximum(jnp.sqrt(norm_square), bound)
    scale_terms = by_micro(is_last, own_scales, swapped(own_scales, "pipe"))

    first_blocks, group_scales = column_blocks(first_pieces, first_order, group_count, column_part, own_scales)
    first_blocks_other = swapped(first_blocks, "pipe")
    all_scales = by_micro(is_last, group_scales, swapped(group_scales, "pipe"))

    grad_blocks = jnp.where(
        is_last,
        by_micro(is_last, last_blocks, last_blocks_other),
        by_micro(is_last, first_blocks, first_blocks_other),
    )
    row_scales = jnp.where(is_last, all_scales, jnp.ones_like(all_scales))
    scaled_blocks = (
        grad_blocks.reshape(micro_count, group_count, example_count, length_count, column_part).astype(
            jnp.float32
        )
        * row_scales.reshape(micro_count, group_count, example_count)[:, :, :, None, None]
    ).astype(jnp.bfloat16)
    flat_inputs = gathered_inputs.reshape(micro_count * group_count * token_count, width_part)
    flat_grads = scaled_blocks.reshape(micro_count * group_count * token_count, column_part)
    summed_grad = lax.dot_general(
        flat_inputs, flat_grads, (((0,), (0,)), ((), ())), preferred_element_type=jnp.float32
    )
    noise_weight = 1.5 / full_width
    per_example_sum = micro_count * group_count * example_count
    final_output = (
        summed_grad + noise_weight * bound * noise[0].astype(jnp.float32)
    ) / per_example_sum
    return (final_output[None], scale_terms)


def solution(mesh):
    in_specs = (
        P("pipe", "tensor", "dp"),
        P("pipe", None, "dp", None, "tensor"),
        P(None, "dp", None, "tensor"),
        P(),
        P("pipe", "tensor", "dp"),
    )
    out_specs = (P("pipe", "tensor", "dp"), P(None, "dp"))
    return jax.shard_map(local, mesh=mesh, in_specs=in_specs, out_specs=out_specs, check_vma=False)
```

```python
import jax
import jax.numpy as jnp
from jax import lax
from jax.sharding import PartitionSpec as P


def swapped(value, axis):
    count = lax.axis_size(axis)
    return lax.ppermute(value, axis, [(source, count - 1 - source) for source in range(count)])


def ring_pieces(values, axis):
    count = lax.axis_size(axis)
    position = lax.axis_index(axis)
    pieces = [values]
    for offset in range(1, count):
        pieces.append(
            lax.ppermute(values, axis, [(source, (source + offset) % count) for source in range(count)])
        )
    stacked = jnp.stack(pieces)
    return stacked, (position - jnp.arange(count)) % count


def feature_pieces(values):
    stacked, order = ring_pieces(values, "tensor")
    grams = jnp.einsum("jeld,jekd->elk", stacked, stacked, preferred_element_type=jnp.float32)
    return stacked, order, grams


def column_blocks(stacked, order, group_count, column_part, row_scales=None):
    pieces, example_count, length_count, width_part = stacked.shape
    token_count = example_count * length_count
    if row_scales is not None:
        stacked = (stacked.astype(jnp.float32) * row_scales[None, :, None, None]).astype(jnp.bfloat16)
    per_piece = width_part // column_part
    chunks = stacked.reshape(pieces, token_count, per_piece, column_part).transpose(0, 2, 1, 3)
    chunks = jnp.take(chunks, order, axis=0).reshape(pieces * per_piece, token_count, column_part)
    extra = 0
    if row_scales is not None:
        parts = []
        rest = row_scales
        for _ in range(3):
            part = lax.optimization_barrier(rest.astype(jnp.bfloat16))
            parts.append(part)
            rest = rest - part.astype(jnp.float32)
        extra = 16
        rows = jnp.zeros((extra, column_part), jnp.bfloat16)
        rows = rows.at[: len(parts), :example_count].set(jnp.stack(parts))
        rows = jnp.broadcast_to(rows[None], (pieces * per_piece, extra, column_part))
        chunks = jnp.concatenate([chunks, rows], axis=1)
    moved = lax.all_to_all(chunks, "dp", split_axis=0, concat_axis=1, tiled=True)
    moved = moved.reshape(group_count, token_count + extra, column_part)
    blocks = moved[:, :token_count].reshape(group_count * token_count, column_part)
    if row_scales is None:
        return blocks
    received = moved[:, token_count : token_count + 3, :example_count].astype(jnp.float32)
    return blocks, (received[:, 2] + received[:, 1]) + received[:, 0]


def token_grams(values):
    return jnp.einsum("...ld,...kd->...lk", values, values, preferred_element_type=jnp.float32)


def by_micro(is_last, own, other):
    return jnp.where(is_last, jnp.stack([other, own]), jnp.stack([own, other]))


def local(weights, inputs, cotangent, clip_norm, noise):
    section_index = lax.axis_index("pipe")
    group_count = lax.axis_size("dp")
    weight_block = weights[0]
    local_inputs = inputs[0]
    micro_count, example_count, length_count, width_part = local_inputs.shape
    token_count = example_count * length_count
    column_part = weight_block.shape[1]
    full_width = column_part * group_count
    is_last = section_index == 1

    gathered_inputs = lax.all_gather(local_inputs, "dp", axis=1, tiled=True)
    input_grams = lax.psum(token_grams(local_inputs), "tensor")

    own_cotangent = lax.dynamic_index_in_dim(cotangent, section_index, 0, keepdims=False)
    last_pieces, last_order, last_grams = feature_pieces(own_cotangent)
    last_blocks = column_blocks(last_pieces, last_order, group_count, column_part)
    last_blocks_other = swapped(last_blocks, "pipe")

    last_weights = jnp.where(is_last, weight_block, swapped(weight_block, "pipe"))
    terms = lax.dot_general(
        last_blocks, last_weights, (((1,), (1,)), ((), ())), preferred_element_type=jnp.float32
    ).astype(jnp.bfloat16)
    terms, input_grams = lax.optimization_barrier((terms, input_grams))
    summed = lax.psum_scatter(terms, "dp", scatter_dimension=0, tiled=True).astype(jnp.float32)
    other_input_grams = swapped(input_grams, "pipe")
    renewed = (own_cotangent.reshape(token_count, width_part).astype(jnp.float32) + summed).astype(
        jnp.bfloat16
    ).reshape(example_count, length_count, width_part)
    first_pieces, first_order, first_grams = feature_pieces(renewed)

    own_input_grams = lax.dynamic_index_in_dim(input_grams, section_index, 0, keepdims=False)
    held_input_grams = lax.dynamic_index_in_dim(other_input_grams, section_index, 0, keepdims=False)
    last_input_grams = jnp.where(is_last, own_input_grams, held_input_grams)
    first_input_grams = jnp.where(is_last, held_input_grams, own_input_grams)
    norm_square = jnp.sum(first_input_grams * first_grams, axis=(1, 2)) + jnp.sum(
        last_input_grams * last_grams, axis=(1, 2)
    )
    bound = clip_norm[0]
    own_scales = bound / jnp.maximum(jnp.sqrt(norm_square), bound)
    scale_terms = by_micro(is_last, own_scales, swapped(own_scales, "pipe"))

    first_blocks, group_scales = column_blocks(first_pieces, first_order, group_count, column_part, own_scales)
    first_blocks_other = swapped(first_blocks, "pipe")
    all_scales = by_micro(is_last, group_scales, swapped(group_scales, "pipe"))

    grad_blocks = jnp.where(
        is_last,
        by_micro(is_last, last_blocks, last_blocks_other),
        by_micro(is_last, first_blocks, first_blocks_other),
    )
    row_scales = jnp.where(is_last, all_scales, jnp.ones_like(all_scales))
    scaled_blocks = (
        grad_blocks.reshape(micro_count, group_count, example_count, length_count, column_part).astype(
            jnp.float32
        )
        * row_scales.reshape(micro_count, group_count, example_count)[:, :, :, None, None]
    ).astype(jnp.bfloat16)
    flat_inputs = gathered_inputs.reshape(micro_count * group_count * token_count, width_part)
    flat_grads = scaled_blocks.reshape(micro_count * group_count * token_count, column_part)
    summed_grad = lax.dot_general(
        flat_inputs, flat_grads, (((0,), (0,)), ((), ())), preferred_element_type=jnp.float32
    )
    noise_weight = 1.5 / full_width
    per_example_sum = micro_count * group_count * example_count
    final_output = (
        summed_grad + noise_weight * bound * noise[0].astype(jnp.float32)
    ) / per_example_sum
    return (final_output[None], scale_terms)


def solution(mesh):
    in_specs = (
        P("pipe", "tensor", "dp"),
        P("pipe", None, "dp", None, "tensor"),
        P(None, "dp", None, "tensor"),
        P(),
        P("pipe", "tensor", "dp"),
    )
    out_specs = (P("pipe", "tensor", "dp"), P(None, "dp"))
    return jax.shard_map(local, mesh=mesh, in_specs=in_specs, out_specs=out_specs, check_vma=False)
```

```python
import jax
import jax.numpy as jnp
from jax import lax
from jax.sharding import PartitionSpec as P


def swapped(value, axis):
    count = lax.axis_size(axis)
    return lax.ppermute(value, axis, [(source, count - 1 - source) for source in range(count)])


def ring_pieces(values, axis):
    count = lax.axis_size(axis)
    position = lax.axis_index(axis)
    pieces = [values]
    for offset in range(1, count):
        pieces.append(
            lax.ppermute(values, axis, [(source, (source + offset) % count) for source in range(count)])
        )
    stacked = jnp.stack(pieces)
    return stacked, (position - jnp.arange(count)) % count


def feature_pieces(values):
    stacked, order = ring_pieces(values, "tensor")
    grams = jnp.einsum("jeld,jekd->elk", stacked, stacked, preferred_element_type=jnp.float32)
    return stacked, order, grams


def column_blocks(stacked, order, group_count, column_part, row_scales=None):
    pieces, example_count, length_count, width_part = stacked.shape
    token_count = example_count * length_count
    if row_scales is not None:
        stacked = (stacked.astype(jnp.float32) * row_scales[None, :, None, None]).astype(jnp.bfloat16)
    per_piece = width_part // column_part
    chunks = stacked.reshape(pieces, token_count, per_piece, column_part).transpose(0, 2, 1, 3)
    chunks = jnp.take(chunks, order, axis=0).reshape(pieces * per_piece, token_count, column_part)
    extra = 0
    if row_scales is not None:
        parts = []
        rest = row_scales
        for _ in range(3):
            part = lax.optimization_barrier(rest.astype(jnp.bfloat16))
            parts.append(part)
            rest = rest - part.astype(jnp.float32)
        extra = 16
        rows = jnp.zeros((extra, column_part), jnp.bfloat16)
        rows = rows.at[: len(parts), :example_count].set(jnp.stack(parts))
        rows = jnp.broadcast_to(rows[None], (pieces * per_piece, extra, column_part))
        chunks = jnp.concatenate([chunks, rows], axis=1)
    moved = lax.all_to_all(chunks, "dp", split_axis=0, concat_axis=1, tiled=True)
    moved = moved.reshape(group_count, token_count + extra, column_part)
    blocks = moved[:, :token_count].reshape(group_count * token_count, column_part)
    if row_scales is None:
        return blocks
    received = moved[:, token_count : token_count + 3, :example_count].astype(jnp.float32)
    return blocks, (received[:, 2] + received[:, 1]) + received[:, 0]


def token_grams(values):
    return jnp.einsum("...ld,...kd->...lk", values, values, preferred_element_type=jnp.float32)


def by_micro(is_last, own, other):
    return jnp.where(is_last, jnp.stack([other, own]), jnp.stack([own, other]))


def local(weights, inputs, cotangent, clip_norm, noise):
    section_index = lax.axis_index("pipe")
    group_count = lax.axis_size("dp")
    weight_block = weights[0]
    local_inputs = inputs[0]
    micro_count, example_count, length_count, width_part = local_inputs.shape
    token_count = example_count * length_count
    column_part = weight_block.shape[1]
    full_width = column_part * group_count
    is_last = section_index == 1

    gathered_inputs = lax.all_gather(local_inputs, "dp", axis=1, tiled=True)
    input_grams = lax.psum(token_grams(local_inputs), "tensor")

    own_cotangent = lax.dynamic_index_in_dim(cotangent, section_index, 0, keepdims=False)
    last_pieces, last_order, last_grams = feature_pieces(own_cotangent)
    last_blocks = column_blocks(last_pieces, last_order, group_count, column_part)
    last_blocks_other = swapped(last_blocks, "pipe")

    last_weights = jnp.where(is_last, weight_block, swapped(weight_block, "pipe"))
    terms = lax.dot_general(
        last_blocks, last_weights, (((1,), (1,)), ((), ())), preferred_element_type=jnp.float32
    ).astype(jnp.bfloat16)
    arrived = lax.all_to_all(
        terms.reshape(group_count, token_count, width_part), "dp", split_axis=0, concat_axis=0, tiled=True
    )
    summed = jnp.sum(arrived.astype(jnp.float32), axis=0)
    other_input_grams = swapped(input_grams, "pipe")
    renewed = (own_cotangent.reshape(token_count, width_part).astype(jnp.float32) + summed).astype(
        jnp.bfloat16
    ).reshape(example_count, length_count, width_part)
    first_pieces, first_order, first_grams = feature_pieces(renewed)

    own_input_grams = lax.dynamic_index_in_dim(input_grams, section_index, 0, keepdims=False)
    held_input_grams = lax.dynamic_index_in_dim(other_input_grams, section_index, 0, keepdims=False)
    last_input_grams = jnp.where(is_last, own_input_grams, held_input_grams)
    first_input_grams = jnp.where(is_last, held_input_grams, own_input_grams)
    norm_square = jnp.sum(first_input_grams * first_grams, axis=(1, 2)) + jnp.sum(
        last_input_grams * last_grams, axis=(1, 2)
    )
    bound = clip_norm[0]
    own_scales = bound / jnp.maximum(jnp.sqrt(norm_square), bound)
    scale_terms = by_micro(is_last, own_scales, swapped(own_scales, "pipe"))

    first_blocks, group_scales = column_blocks(first_pieces, first_order, group_count, column_part, own_scales)
    first_blocks_other = swapped(first_blocks, "pipe")
    all_scales = by_micro(is_last, group_scales, swapped(group_scales, "pipe"))

    grad_blocks = jnp.where(
        is_last,
        by_micro(is_last, last_blocks, last_blocks_other),
        by_micro(is_last, first_blocks, first_blocks_other),
    )
    row_scales = jnp.where(is_last, all_scales, jnp.ones_like(all_scales))
    scaled_blocks = (
        grad_blocks.reshape(micro_count, group_count, example_count, length_count, column_part).astype(
            jnp.float32
        )
        * row_scales.reshape(micro_count, group_count, example_count)[:, :, :, None, None]
    ).astype(jnp.bfloat16)
    flat_inputs = gathered_inputs.reshape(micro_count * group_count * token_count, width_part)
    flat_grads = scaled_blocks.reshape(micro_count * group_count * token_count, column_part)
    summed_grad = lax.dot_general(
        flat_inputs, flat_grads, (((0,), (0,)), ((), ())), preferred_element_type=jnp.float32
    )
    noise_weight = 1.5 / full_width
    per_example_sum = micro_count * group_count * example_count
    final_output = (
        summed_grad + noise_weight * bound * noise[0].astype(jnp.float32)
    ) / per_example_sum
    return (final_output[None], scale_terms)


def solution(mesh):
    in_specs = (
        P("pipe", "tensor", "dp"),
        P("pipe", None, "dp", None, "tensor"),
        P(None, "dp", None, "tensor"),
        P(),
        P("pipe", "tensor", "dp"),
    )
    out_specs = (P("pipe", "tensor", "dp"), P(None, "dp"))
    return jax.shard_map(local, mesh=mesh, in_specs=in_specs, out_specs=out_specs, check_vma=False)
```

```python
import jax
import jax.numpy as jnp
from jax import lax
from jax.sharding import PartitionSpec as P


DATA = ("dy", "dx")


def swapped(value, axis):
    count = lax.axis_size(axis)
    return lax.ppermute(value, axis, [(source, count - 1 - source) for source in range(count)])


def ring_pieces(values, axis):
    count = lax.axis_size(axis)
    position = lax.axis_index(axis)
    pieces = [values]
    for offset in range(1, count):
        pieces.append(
            lax.ppermute(values, axis, [(source, (source + offset) % count) for source in range(count)])
        )
    stacked = jnp.stack(pieces)
    return stacked, (position - jnp.arange(count)) % count


def feature_pieces(values):
    stacked, order = ring_pieces(values, "tensor")
    grams = jnp.einsum("jeld,jekd->elk", stacked, stacked, preferred_element_type=jnp.float32)
    return stacked, order, grams


def column_blocks(stacked, order, group_count, column_part, row_scales=None):
    pieces, example_count, length_count, width_part = stacked.shape
    token_count = example_count * length_count
    if row_scales is not None:
        stacked = (stacked.astype(jnp.float32) * row_scales[None, :, None, None]).astype(jnp.bfloat16)
    per_piece = width_part // column_part
    chunks = stacked.reshape(pieces, token_count, per_piece, column_part).transpose(0, 2, 1, 3)
    chunks = jnp.take(chunks, order, axis=0).reshape(pieces * per_piece, token_count, column_part)
    extra = 0
    if row_scales is not None:
        parts = []
        rest = row_scales
        for _ in range(3):
            part = lax.optimization_barrier(rest.astype(jnp.bfloat16))
            parts.append(part)
            rest = rest - part.astype(jnp.float32)
        extra = 16
        rows = jnp.zeros((extra, column_part), jnp.bfloat16)
        rows = rows.at[: len(parts), :example_count].set(jnp.stack(parts))
        rows = jnp.broadcast_to(rows[None], (pieces * per_piece, extra, column_part))
        chunks = jnp.concatenate([chunks, rows], axis=1)
    moved = lax.all_to_all(chunks, DATA, split_axis=0, concat_axis=1, tiled=True)
    moved = moved.reshape(group_count, token_count + extra, column_part)
    blocks = moved[:, :token_count].reshape(group_count * token_count, column_part)
    if row_scales is None:
        return blocks
    received = moved[:, token_count : token_count + 3, :example_count].astype(jnp.float32)
    return blocks, (received[:, 2] + received[:, 1]) + received[:, 0]


def token_grams(values):
    return jnp.einsum("...ld,...kd->...lk", values, values, preferred_element_type=jnp.float32)


def by_micro(is_last, own, other):
    return jnp.where(is_last, jnp.stack([other, own]), jnp.stack([own, other]))


def local(weights, inputs, cotangent, clip_norm, noise):
    section_index = lax.axis_index("pipe")
    group_count = lax.axis_size("dy") * lax.axis_size("dx")
    weight_block = weights[0]
    local_inputs = inputs[0]
    micro_count, example_count, length_count, width_part = local_inputs.shape
    token_count = example_count * length_count
    column_part = weight_block.shape[1]
    full_width = column_part * group_count
    is_last = section_index == 1

    gathered_inputs = lax.all_gather(
        lax.all_gather(local_inputs, "dx", axis=1, tiled=True), "dy", axis=1, tiled=True
    )
    input_grams = lax.psum(token_grams(local_inputs), "tensor")

    own_cotangent = lax.dynamic_index_in_dim(cotangent, section_index, 0, keepdims=False)
    last_pieces, last_order, last_grams = feature_pieces(own_cotangent)
    last_blocks = column_blocks(last_pieces, last_order, group_count, column_part)
    last_blocks_other = swapped(last_blocks, "pipe")

    last_weights = jnp.where(is_last, weight_block, swapped(weight_block, "pipe"))
    terms = lax.dot_general(
        last_blocks, last_weights, (((1,), (1,)), ((), ())), preferred_element_type=jnp.float32
    ).astype(jnp.bfloat16)
    terms, input_grams = lax.optimization_barrier((terms, input_grams))
    summed = lax.psum_scatter(terms, DATA, scatter_dimension=0, tiled=True).astype(jnp.float32)
    other_input_grams = swapped(input_grams, "pipe")
    renewed = (own_cotangent.reshape(token_count, width_part).astype(jnp.float32) + summed).astype(
        jnp.bfloat16
    ).reshape(example_count, length_count, width_part)
    first_pieces, first_order, first_grams = feature_pieces(renewed)

    own_input_grams = lax.dynamic_index_in_dim(input_grams, section_index, 0, keepdims=False)
    held_input_grams = lax.dynamic_index_in_dim(other_input_grams, section_index, 0, keepdims=False)
    last_input_grams = jnp.where(is_last, own_input_grams, held_input_grams)
    first_input_grams = jnp.where(is_last, held_input_grams, own_input_grams)
    norm_square = jnp.sum(first_input_grams * first_grams, axis=(1, 2)) + jnp.sum(
        last_input_grams * last_grams, axis=(1, 2)
    )
    bound = clip_norm[0]
    own_scales = bound / jnp.maximum(jnp.sqrt(norm_square), bound)
    scale_terms = by_micro(is_last, own_scales, swapped(own_scales, "pipe"))

    first_blocks, group_scales = column_blocks(first_pieces, first_order, group_count, column_part, own_scales)
    first_blocks_other = swapped(first_blocks, "pipe")
    all_scales = by_micro(is_last, group_scales, swapped(group_scales, "pipe"))

    grad_blocks = jnp.where(
        is_last,
        by_micro(is_last, last_blocks, last_blocks_other),
        by_micro(is_last, first_blocks, first_blocks_other),
    )
    row_scales = jnp.where(is_last, all_scales, jnp.ones_like(all_scales))
    scaled_blocks = (
        grad_blocks.reshape(micro_count, group_count, example_count, length_count, column_part).astype(
            jnp.float32
        )
        * row_scales.reshape(micro_count, group_count, example_count)[:, :, :, None, None]
    ).astype(jnp.bfloat16)
    flat_inputs = gathered_inputs.reshape(micro_count * group_count * token_count, width_part)
    flat_grads = scaled_blocks.reshape(micro_count * group_count * token_count, column_part)
    summed_grad = lax.dot_general(
        flat_inputs, flat_grads, (((0,), (0,)), ((), ())), preferred_element_type=jnp.float32
    )
    noise_weight = 1.5 / full_width
    per_example_sum = micro_count * group_count * example_count
    final_output = (
        summed_grad + noise_weight * bound * noise[0].astype(jnp.float32)
    ) / per_example_sum
    return (final_output[None], scale_terms)


def solution(mesh):
    sizes = dict(zip(mesh.axis_names, mesh.devices.shape))
    rows = 4 if sizes["dp"] % 4 == 0 else 1
    split_mesh = jax.sharding.Mesh(
        mesh.devices.reshape(sizes["pipe"], rows, sizes["dp"] // rows, sizes["tensor"]),
        ("pipe", "dy", "dx", "tensor"),
    )
    in_specs = (
        P("pipe", "tensor", DATA),
        P("pipe", None, DATA, None, "tensor"),
        P(None, DATA, None, "tensor"),
        P(),
        P("pipe", "tensor", DATA),
    )
    out_specs = (P("pipe", "tensor", DATA), P(None, DATA))
    return jax.shard_map(local, mesh=split_mesh, in_specs=in_specs, out_specs=out_specs, check_vma=False)
```

```python
import jax
import jax.numpy as jnp
from jax import lax
from jax.sharding import PartitionSpec as P


def swapped(value, axis):
    count = lax.axis_size(axis)
    return lax.ppermute(value, axis, [(source, count - 1 - source) for source in range(count)])


def ring_pieces(values, axis):
    count = lax.axis_size(axis)
    position = lax.axis_index(axis)
    pieces = [values]
    for offset in range(1, count):
        pieces.append(
            lax.ppermute(values, axis, [(source, (source + offset) % count) for source in range(count)])
        )
    stacked = jnp.stack(pieces)
    return stacked, (position - jnp.arange(count)) % count


def feature_pieces(values):
    stacked, order = ring_pieces(values, "tensor")
    grams = jnp.einsum("jeld,jekd->elk", stacked, stacked, preferred_element_type=jnp.float32)
    return stacked, order, grams


def column_blocks(stacked, order, group_count, column_part, row_scales=None):
    pieces, example_count, length_count, width_part = stacked.shape
    token_count = example_count * length_count
    if row_scales is not None:
        stacked = (stacked.astype(jnp.float32) * row_scales[None, :, None, None]).astype(jnp.bfloat16)
    per_piece = width_part // column_part
    chunks = stacked.reshape(pieces, token_count, per_piece, column_part).transpose(0, 2, 1, 3)
    chunks = jnp.take(chunks, order, axis=0).reshape(pieces * per_piece, token_count, column_part)
    extra = 0
    if row_scales is not None:
        parts = []
        rest = row_scales
        for _ in range(3):
            part = lax.optimization_barrier(rest.astype(jnp.bfloat16))
            parts.append(part)
            rest = rest - part.astype(jnp.float32)
        extra = 16
        rows = jnp.zeros((extra, column_part), jnp.bfloat16)
        rows = rows.at[: len(parts), :example_count].set(jnp.stack(parts))
        rows = jnp.broadcast_to(rows[None], (pieces * per_piece, extra, column_part))
        chunks = jnp.concatenate([chunks, rows], axis=1)
    moved = lax.all_to_all(chunks, "dp", split_axis=0, concat_axis=1, tiled=True)
    moved = moved.reshape(group_count, token_count + extra, column_part)
    blocks = moved[:, :token_count].reshape(group_count * token_count, column_part)
    if row_scales is None:
        return blocks
    received = moved[:, token_count : token_count + 3, :example_count].astype(jnp.float32)
    return blocks, (received[:, 2] + received[:, 1]) + received[:, 0]


def token_grams(values):
    return jnp.einsum("...ld,...kd->...lk", values, values, preferred_element_type=jnp.float32)


def by_micro(is_last, own, other):
    return jnp.where(is_last, jnp.stack([other, own]), jnp.stack([own, other]))


def local(weights, inputs, cotangent, clip_norm, noise):
    section_index = lax.axis_index("pipe")
    group_count = lax.axis_size("dp")
    weight_block = weights[0]
    local_inputs = inputs[0]
    micro_count, example_count, length_count, width_part = local_inputs.shape
    token_count = example_count * length_count
    column_part = weight_block.shape[1]
    full_width = column_part * group_count
    is_last = section_index == 1

    early_inputs = lax.all_gather(local_inputs[:1], "dp", axis=1, tiled=True)
    input_grams = lax.psum(token_grams(local_inputs), "tensor")

    own_cotangent = lax.dynamic_index_in_dim(cotangent, section_index, 0, keepdims=False)
    last_pieces, last_order, last_grams = feature_pieces(own_cotangent)
    last_blocks = column_blocks(last_pieces, last_order, group_count, column_part)
    last_blocks_other = swapped(last_blocks, "pipe")

    last_weights = jnp.where(is_last, weight_block, swapped(weight_block, "pipe"))
    terms = lax.dot_general(
        last_blocks, last_weights, (((1,), (1,)), ((), ())), preferred_element_type=jnp.float32
    ).astype(jnp.bfloat16)
    terms, input_grams, early_inputs = lax.optimization_barrier((terms, input_grams, early_inputs))
    summed = lax.psum_scatter(terms, "dp", scatter_dimension=0, tiled=True).astype(jnp.float32)
    late_inputs = lax.all_gather(local_inputs[1:], "dp", axis=1, tiled=True)
    gathered_inputs = jnp.concatenate([early_inputs, late_inputs], axis=0)
    other_input_grams = swapped(input_grams, "pipe")
    renewed = (own_cotangent.reshape(token_count, width_part).astype(jnp.float32) + summed).astype(
        jnp.bfloat16
    ).reshape(example_count, length_count, width_part)
    first_pieces, first_order, first_grams = feature_pieces(renewed)

    own_input_grams = lax.dynamic_index_in_dim(input_grams, section_index, 0, keepdims=False)
    held_input_grams = lax.dynamic_index_in_dim(other_input_grams, section_index, 0, keepdims=False)
    last_input_grams = jnp.where(is_last, own_input_grams, held_input_grams)
    first_input_grams = jnp.where(is_last, held_input_grams, own_input_grams)
    norm_square = jnp.sum(first_input_grams * first_grams, axis=(1, 2)) + jnp.sum(
        last_input_grams * last_grams, axis=(1, 2)
    )
    bound = clip_norm[0]
    own_scales = bound / jnp.maximum(jnp.sqrt(norm_square), bound)
    scale_terms = by_micro(is_last, own_scales, swapped(own_scales, "pipe"))

    first_blocks, group_scales = column_blocks(first_pieces, first_order, group_count, column_part, own_scales)
    first_blocks_other = swapped(first_blocks, "pipe")
    all_scales = by_micro(is_last, group_scales, swapped(group_scales, "pipe"))

    grad_blocks = jnp.where(
        is_last,
        by_micro(is_last, last_blocks, last_blocks_other),
        by_micro(is_last, first_blocks, first_blocks_other),
    )
    row_scales = jnp.where(is_last, all_scales, jnp.ones_like(all_scales))
    scaled_blocks = (
        grad_blocks.reshape(micro_count, group_count, example_count, length_count, column_part).astype(
            jnp.float32
        )
        * row_scales.reshape(micro_count, group_count, example_count)[:, :, :, None, None]
    ).astype(jnp.bfloat16)
    flat_inputs = gathered_inputs.reshape(micro_count * group_count * token_count, width_part)
    flat_grads = scaled_blocks.reshape(micro_count * group_count * token_count, column_part)
    summed_grad = lax.dot_general(
        flat_inputs, flat_grads, (((0,), (0,)), ((), ())), preferred_element_type=jnp.float32
    )
    noise_weight = 1.5 / full_width
    per_example_sum = micro_count * group_count * example_count
    final_output = (
        summed_grad + noise_weight * bound * noise[0].astype(jnp.float32)
    ) / per_example_sum
    return (final_output[None], scale_terms)


def solution(mesh):
    in_specs = (
        P("pipe", "tensor", "dp"),
        P("pipe", None, "dp", None, "tensor"),
        P(None, "dp", None, "tensor"),
        P(),
        P("pipe", "tensor", "dp"),
    )
    out_specs = (P("pipe", "tensor", "dp"), P(None, "dp"))
    return jax.shard_map(local, mesh=mesh, in_specs=in_specs, out_specs=out_specs, check_vma=False)
```

```python
import jax
import jax.numpy as jnp
from jax import lax
from jax.sharding import PartitionSpec as P


def swapped(value, axis):
    count = lax.axis_size(axis)
    return lax.ppermute(value, axis, [(source, count - 1 - source) for source in range(count)])


def ring_pieces(values, axis):
    count = lax.axis_size(axis)
    position = lax.axis_index(axis)
    pieces = [values]
    for offset in range(1, count):
        pieces.append(
            lax.ppermute(values, axis, [(source, (source + offset) % count) for source in range(count)])
        )
    stacked = jnp.stack(pieces)
    return stacked, (position - jnp.arange(count)) % count


def feature_pieces(values):
    stacked, order = ring_pieces(values, "tensor")
    grams = jnp.einsum("jeld,jekd->elk", stacked, stacked, preferred_element_type=jnp.float32)
    return stacked, order, grams


def column_blocks(stacked, order, group_count, column_part, row_scales=None):
    pieces, example_count, length_count, width_part = stacked.shape
    token_count = example_count * length_count
    if row_scales is not None:
        stacked = (stacked.astype(jnp.float32) * row_scales[None, :, None, None]).astype(jnp.bfloat16)
    per_piece = width_part // column_part
    chunks = stacked.reshape(pieces, token_count, per_piece, column_part).transpose(0, 2, 1, 3)
    chunks = jnp.take(chunks, order, axis=0).reshape(pieces * per_piece, token_count, column_part)
    extra = 0
    if row_scales is not None:
        parts = []
        rest = row_scales
        for _ in range(3):
            part = lax.optimization_barrier(rest.astype(jnp.bfloat16))
            parts.append(part)
            rest = rest - part.astype(jnp.float32)
        extra = 16
        rows = jnp.zeros((extra, column_part), jnp.bfloat16)
        rows = rows.at[: len(parts), :example_count].set(jnp.stack(parts))
        rows = jnp.broadcast_to(rows[None], (pieces * per_piece, extra, column_part))
        chunks = jnp.concatenate([chunks, rows], axis=1)
    moved = lax.all_to_all(chunks, "dp", split_axis=0, concat_axis=1, tiled=True)
    moved = moved.reshape(group_count, token_count + extra, column_part)
    blocks = moved[:, :token_count].reshape(group_count * token_count, column_part)
    if row_scales is None:
        return blocks
    received = moved[:, token_count : token_count + 3, :example_count].astype(jnp.float32)
    return blocks, (received[:, 2] + received[:, 1]) + received[:, 0]


def token_grams(values):
    return jnp.einsum("...ld,...kd->...lk", values, values, preferred_element_type=jnp.float32)


def by_micro(is_last, own, other):
    return jnp.where(is_last, jnp.stack([other, own]), jnp.stack([own, other]))


def local(weights, inputs, cotangent, clip_norm, noise):
    section_index = lax.axis_index("pipe")
    group_count = lax.axis_size("dp")
    weight_block = weights[0]
    local_inputs = inputs[0]
    micro_count, example_count, length_count, width_part = local_inputs.shape
    token_count = example_count * length_count
    column_part = weight_block.shape[1]
    full_width = column_part * group_count
    is_last = section_index == 1

    early_inputs = lax.all_gather(local_inputs[:1], "dp", axis=1, tiled=True)
    input_grams = lax.psum(token_grams(local_inputs), "tensor")

    own_cotangent = lax.dynamic_index_in_dim(cotangent, section_index, 0, keepdims=False)
    last_pieces, last_order, last_grams = feature_pieces(own_cotangent)
    last_blocks = column_blocks(last_pieces, last_order, group_count, column_part)
    last_blocks_other = swapped(last_blocks, "pipe")

    last_weights = jnp.where(is_last, weight_block, swapped(weight_block, "pipe"))
    terms = lax.dot_general(
        last_blocks, last_weights, (((1,), (1,)), ((), ())), preferred_element_type=jnp.float32
    ).astype(jnp.bfloat16)
    terms, input_grams, early_inputs = lax.optimization_barrier((terms, input_grams, early_inputs))
    summed = lax.psum_scatter(terms, "dp", scatter_dimension=0, tiled=True).astype(jnp.float32)
    late_inputs = lax.all_gather(local_inputs[1:], "dp", axis=1, tiled=True)
    other_input_grams = swapped(input_grams, "pipe")
    renewed = (own_cotangent.reshape(token_count, width_part).astype(jnp.float32) + summed).astype(
        jnp.bfloat16
    ).reshape(example_count, length_count, width_part)
    first_pieces, first_order, first_grams = feature_pieces(renewed)

    own_input_grams = lax.dynamic_index_in_dim(input_grams, section_index, 0, keepdims=False)
    held_input_grams = lax.dynamic_index_in_dim(other_input_grams, section_index, 0, keepdims=False)
    last_input_grams = jnp.where(is_last, own_input_grams, held_input_grams)
    first_input_grams = jnp.where(is_last, held_input_grams, own_input_grams)
    norm_square = jnp.sum(first_input_grams * first_grams, axis=(1, 2)) + jnp.sum(
        last_input_grams * last_grams, axis=(1, 2)
    )
    bound = clip_norm[0]
    own_scales = bound / jnp.maximum(jnp.sqrt(norm_square), bound)
    scale_terms = by_micro(is_last, own_scales, swapped(own_scales, "pipe"))

    first_blocks, group_scales = column_blocks(first_pieces, first_order, group_count, column_part, own_scales)
    first_blocks_other = swapped(first_blocks, "pipe")
    all_scales = by_micro(is_last, group_scales, swapped(group_scales, "pipe"))

    grad_blocks = jnp.where(
        is_last,
        by_micro(is_last, last_blocks, last_blocks_other),
        by_micro(is_last, first_blocks, first_blocks_other),
    )
    row_scales = jnp.where(is_last, all_scales, jnp.ones_like(all_scales))
    scaled_blocks = (
        grad_blocks.reshape(micro_count, group_count, example_count, length_count, column_part).astype(
            jnp.float32
        )
        * row_scales.reshape(micro_count, group_count, example_count)[:, :, :, None, None]
    ).astype(jnp.bfloat16)
    summed_grad = sum(
        lax.dot_general(
            half.reshape(group_count * token_count, width_part),
            scaled_blocks[index].reshape(group_count * token_count, column_part),
            (((0,), (0,)), ((), ())),
            preferred_element_type=jnp.float32,
        )
        for index, half in enumerate([early_inputs[0], late_inputs[0]])
    )
    noise_weight = 1.5 / full_width
    per_example_sum = micro_count * group_count * example_count
    final_output = (
        summed_grad + noise_weight * bound * noise[0].astype(jnp.float32)
    ) / per_example_sum
    return (final_output[None], scale_terms)


def solution(mesh):
    in_specs = (
        P("pipe", "tensor", "dp"),
        P("pipe", None, "dp", None, "tensor"),
        P(None, "dp", None, "tensor"),
        P(),
        P("pipe", "tensor", "dp"),
    )
    out_specs = (P("pipe", "tensor", "dp"), P(None, "dp"))
    return jax.shard_map(local, mesh=mesh, in_specs=in_specs, out_specs=out_specs, check_vma=False)
```

```python
import jax
import jax.numpy as jnp
from jax import lax
from jax.sharding import PartitionSpec as P


def swapped(value, axis):
    count = lax.axis_size(axis)
    return lax.ppermute(value, axis, [(source, count - 1 - source) for source in range(count)])


def ring_pieces(values, axis):
    count = lax.axis_size(axis)
    position = lax.axis_index(axis)
    pieces = [values]
    for offset in range(1, count):
        pieces.append(
            lax.ppermute(values, axis, [(source, (source + offset) % count) for source in range(count)])
        )
    stacked = jnp.stack(pieces)
    return stacked, (position - jnp.arange(count)) % count


def grid_gather(values, group_count):
    columns = 4 if group_count % 4 == 0 else group_count
    rows = group_count // columns
    position = lax.axis_index("dp")

    def along(piece, count, stride):
        pieces = [piece]
        for offset in range(1, count):
            pairs = []
            for source in range(group_count):
                at = (source // stride) % count
                pairs.append((source, source + (((at + offset) % count) - at) * stride))
            pieces.append(lax.ppermute(piece, "dp", pairs))
        order = ((position // stride) % count - jnp.arange(count)) % count
        return jnp.take(jnp.stack(pieces), order, axis=0)

    across = along(values, columns, 1)
    return along(across, rows, columns).reshape((group_count,) + values.shape)


def column_blocks(values, group_count, column_part):
    example_count, length_count, width_part = values.shape
    token_count = example_count * length_count
    stacked, order = ring_pieces(values, "tensor")
    grams = jnp.einsum("jeld,jekd->elk", stacked, stacked, preferred_element_type=jnp.float32)
    pieces = stacked.shape[0]
    per_piece = width_part // column_part
    chunks = stacked.reshape(pieces, token_count, per_piece, column_part).transpose(0, 2, 1, 3)
    chunks = jnp.take(chunks, order, axis=0).reshape(pieces * per_piece, token_count, column_part)
    moved = lax.all_to_all(chunks, "dp", split_axis=0, concat_axis=1, tiled=True)
    return grams, moved.reshape(group_count * token_count, column_part)


def token_grams(values):
    return jnp.einsum("...ld,...kd->...lk", values, values, preferred_element_type=jnp.float32)


def by_micro(is_last, own, other):
    return jnp.where(is_last, jnp.stack([other, own]), jnp.stack([own, other]))


def local(weights, inputs, cotangent, clip_norm, noise):
    section_index = lax.axis_index("pipe")
    group_count = lax.axis_size("dp")
    weight_block = weights[0]
    local_inputs = inputs[0]
    micro_count, example_count, length_count, width_part = local_inputs.shape
    token_count = example_count * length_count
    column_part = weight_block.shape[1]
    full_width = column_part * group_count
    is_last = section_index == 1

    gathered_inputs = lax.all_gather(local_inputs, "dp", axis=1, tiled=True)
    input_grams = lax.psum(token_grams(local_inputs), "tensor")
    other_input_grams = swapped(input_grams, "pipe")

    own_cotangent = lax.dynamic_index_in_dim(cotangent, section_index, 0, keepdims=False)
    last_grams, last_blocks = column_blocks(own_cotangent, group_count, column_part)
    last_blocks_other = swapped(last_blocks, "pipe")

    last_weights = jnp.where(is_last, weight_block, swapped(weight_block, "pipe"))
    terms = lax.dot_general(
        last_blocks, last_weights, (((1,), (1,)), ((), ())), preferred_element_type=jnp.float32
    ).astype(jnp.bfloat16)
    summed = lax.psum_scatter(terms, "dp", scatter_dimension=0, tiled=True).astype(jnp.float32)
    renewed = (own_cotangent.reshape(token_count, width_part).astype(jnp.float32) + summed).astype(
        jnp.bfloat16
    ).reshape(example_count, length_count, width_part)
    first_grams, first_blocks = column_blocks(renewed, group_count, column_part)
    first_blocks_other = swapped(first_blocks, "pipe")

    own_input_grams = lax.dynamic_index_in_dim(input_grams, section_index, 0, keepdims=False)
    held_input_grams = lax.dynamic_index_in_dim(other_input_grams, section_index, 0, keepdims=False)
    last_input_grams = jnp.where(is_last, own_input_grams, held_input_grams)
    first_input_grams = jnp.where(is_last, held_input_grams, own_input_grams)
    norm_square = jnp.sum(first_input_grams * first_grams, axis=(1, 2)) + jnp.sum(
        last_input_grams * last_grams, axis=(1, 2)
    )
    bound = clip_norm[0]
    own_scales = bound / jnp.maximum(jnp.sqrt(norm_square), bound)
    scale_terms = by_micro(is_last, own_scales, swapped(own_scales, "pipe"))
    all_scales = grid_gather(scale_terms, group_count).transpose(1, 0, 2)

    grad_blocks = jnp.where(
        is_last,
        by_micro(is_last, last_blocks, last_blocks_other),
        by_micro(is_last, first_blocks, first_blocks_other),
    )
    scaled_blocks = (
        grad_blocks.reshape(micro_count, group_count, example_count, length_count, column_part).astype(
            jnp.float32
        )
        * all_scales[:, :, :, None, None]
    ).astype(jnp.bfloat16)
    summed_grad = sum(
        lax.dot_general(
            gathered_inputs[index].reshape(group_count * token_count, width_part),
            scaled_blocks[index].reshape(group_count * token_count, column_part),
            (((0,), (0,)), ((), ())),
            preferred_element_type=jnp.float32,
        )
        for index in range(micro_count)
    )
    noise_weight = 1.5 / full_width
    per_example_sum = micro_count * group_count * example_count
    final_output = (
        summed_grad + noise_weight * bound * noise[0].astype(jnp.float32)
    ) / per_example_sum
    return (final_output[None], scale_terms)


def solution(mesh):
    in_specs = (
        P("pipe", "tensor", "dp"),
        P("pipe", None, "dp", None, "tensor"),
        P(None, "dp", None, "tensor"),
        P(),
        P("pipe", "tensor", "dp"),
    )
    out_specs = (P("pipe", "tensor", "dp"), P(None, "dp"))
    return jax.shard_map(local, mesh=mesh, in_specs=in_specs, out_specs=out_specs, check_vma=False)
```

```python
import jax
import jax.numpy as jnp
from jax import lax
from jax.sharding import PartitionSpec as P


def swapped(value, axis):
    count = lax.axis_size(axis)
    return lax.ppermute(value, axis, [(source, count - 1 - source) for source in range(count)])


def ring_pieces(values, axis):
    count = lax.axis_size(axis)
    position = lax.axis_index(axis)
    pieces = [values]
    for offset in range(1, count):
        pieces.append(
            lax.ppermute(values, axis, [(source, (source + offset) % count) for source in range(count)])
        )
    stacked = jnp.stack(pieces)
    return stacked, (position - jnp.arange(count)) % count


def grid_gather(values, group_count):
    columns = 4 if group_count % 4 == 0 else group_count
    rows = group_count // columns
    position = lax.axis_index("dp")

    def along(piece, count, stride):
        pieces = [piece]
        for offset in range(1, count):
            pairs = []
            for source in range(group_count):
                at = (source // stride) % count
                pairs.append((source, source + (((at + offset) % count) - at) * stride))
            pieces.append(lax.ppermute(piece, "dp", pairs))
        order = ((position // stride) % count - jnp.arange(count)) % count
        return jnp.take(jnp.stack(pieces), order, axis=0)

    across = along(values, columns, 1)
    return along(across, rows, columns).reshape((group_count,) + values.shape)


def column_blocks(values, group_count, column_part, before_send=None):
    example_count, length_count, width_part = values.shape
    token_count = example_count * length_count
    stacked, order = ring_pieces(values, "tensor")
    grams = jnp.einsum("jeld,jekd->elk", stacked, stacked, preferred_element_type=jnp.float32)
    pieces = stacked.shape[0]
    per_piece = width_part // column_part
    chunks = stacked.reshape(pieces, token_count, per_piece, column_part).transpose(0, 2, 1, 3)
    chunks = jnp.take(chunks, order, axis=0).reshape(pieces * per_piece, token_count, column_part)
    extra = None
    if before_send is not None:
        extra = before_send(grams)
        chunks, extra = lax.optimization_barrier((chunks, extra))
    moved = lax.all_to_all(chunks, "dp", split_axis=0, concat_axis=1, tiled=True)
    return grams, moved.reshape(group_count * token_count, column_part), extra


def token_grams(values):
    return jnp.einsum("...ld,...kd->...lk", values, values, preferred_element_type=jnp.float32)


def by_micro(is_last, own, other):
    return jnp.where(is_last, jnp.stack([other, own]), jnp.stack([own, other]))


def local(weights, inputs, cotangent, clip_norm, noise):
    section_index = lax.axis_index("pipe")
    group_count = lax.axis_size("dp")
    weight_block = weights[0]
    local_inputs = inputs[0]
    micro_count, example_count, length_count, width_part = local_inputs.shape
    token_count = example_count * length_count
    column_part = weight_block.shape[1]
    full_width = column_part * group_count
    is_last = section_index == 1

    gathered_inputs = lax.all_gather(local_inputs, "dp", axis=1, tiled=True)
    input_grams = lax.psum(token_grams(local_inputs), "tensor")
    other_input_grams = swapped(input_grams, "pipe")

    own_cotangent = lax.dynamic_index_in_dim(cotangent, section_index, 0, keepdims=False)
    last_grams, last_blocks, _ = column_blocks(own_cotangent, group_count, column_part)
    last_blocks_other = swapped(last_blocks, "pipe")

    last_weights = jnp.where(is_last, weight_block, swapped(weight_block, "pipe"))
    terms = lax.dot_general(
        last_blocks, last_weights, (((1,), (1,)), ((), ())), preferred_element_type=jnp.float32
    ).astype(jnp.bfloat16)
    summed = lax.psum_scatter(terms, "dp", scatter_dimension=0, tiled=True).astype(jnp.float32)
    renewed = (own_cotangent.reshape(token_count, width_part).astype(jnp.float32) + summed).astype(
        jnp.bfloat16
    ).reshape(example_count, length_count, width_part)
    own_input_grams = lax.dynamic_index_in_dim(input_grams, section_index, 0, keepdims=False)
    held_input_grams = lax.dynamic_index_in_dim(other_input_grams, section_index, 0, keepdims=False)
    last_input_grams = jnp.where(is_last, own_input_grams, held_input_grams)
    first_input_grams = jnp.where(is_last, held_input_grams, own_input_grams)
    bound = clip_norm[0]

    def clip_factors(first_grams):
        norm_square = jnp.sum(first_input_grams * first_grams, axis=(1, 2)) + jnp.sum(
            last_input_grams * last_grams, axis=(1, 2)
        )
        own_scales = bound / jnp.maximum(jnp.sqrt(norm_square), bound)
        scale_terms = by_micro(is_last, own_scales, swapped(own_scales, "pipe"))
        return scale_terms, grid_gather(scale_terms, group_count).transpose(1, 0, 2)

    _, first_blocks, (scale_terms, all_scales) = column_blocks(renewed, group_count, column_part, clip_factors)
    first_blocks_other = swapped(first_blocks, "pipe")

    grad_blocks = jnp.where(
        is_last,
        by_micro(is_last, last_blocks, last_blocks_other),
        by_micro(is_last, first_blocks, first_blocks_other),
    )
    scaled_blocks = (
        grad_blocks.reshape(micro_count, group_count, example_count, length_count, column_part).astype(
            jnp.float32
        )
        * all_scales[:, :, :, None, None]
    ).astype(jnp.bfloat16)
    summed_grad = sum(
        lax.dot_general(
            gathered_inputs[index].reshape(group_count * token_count, width_part),
            scaled_blocks[index].reshape(group_count * token_count, column_part),
            (((0,), (0,)), ((), ())),
            preferred_element_type=jnp.float32,
        )
        for index in range(micro_count)
    )
    noise_weight = 1.5 / full_width
    per_example_sum = micro_count * group_count * example_count
    final_output = (
        summed_grad + noise_weight * bound * noise[0].astype(jnp.float32)
    ) / per_example_sum
    return (final_output[None], scale_terms)


def solution(mesh):
    in_specs = (
        P("pipe", "tensor", "dp"),
        P("pipe", None, "dp", None, "tensor"),
        P(None, "dp", None, "tensor"),
        P(),
        P("pipe", "tensor", "dp"),
    )
    out_specs = (P("pipe", "tensor", "dp"), P(None, "dp"))
    return jax.shard_map(local, mesh=mesh, in_specs=in_specs, out_specs=out_specs, check_vma=False)
```

```python
import jax
import jax.numpy as jnp
from jax import lax
from jax.sharding import PartitionSpec as P


def swapped(value, axis):
    count = lax.axis_size(axis)
    return lax.ppermute(value, axis, [(source, count - 1 - source) for source in range(count)])


def ring_pieces(values, axis):
    count = lax.axis_size(axis)
    position = lax.axis_index(axis)
    pieces = [values]
    for offset in range(1, count):
        pieces.append(
            lax.ppermute(values, axis, [(source, (source + offset) % count) for source in range(count)])
        )
    stacked = jnp.stack(pieces)
    return stacked, (position - jnp.arange(count)) % count


def column_blocks(values, group_count, column_part):
    example_count, length_count, width_part = values.shape
    token_count = example_count * length_count
    stacked, order = ring_pieces(values, "tensor")
    grams = jnp.einsum("jeld,jekd->elk", stacked, stacked, preferred_element_type=jnp.float32)
    pieces = stacked.shape[0]
    per_piece = width_part // column_part
    chunks = stacked.reshape(pieces, token_count, per_piece, column_part).transpose(0, 2, 1, 3)
    chunks = jnp.take(chunks, order, axis=0).reshape(pieces * per_piece, token_count, column_part)
    moved = lax.all_to_all(chunks, "dp", split_axis=0, concat_axis=1, tiled=True)
    return grams, moved.reshape(group_count * token_count, column_part)


def token_grams(values):
    return jnp.einsum("...ld,...kd->...lk", values, values, preferred_element_type=jnp.float32)


def by_micro(is_last, own, other):
    return jnp.where(is_last, jnp.stack([other, own]), jnp.stack([own, other]))


def local(weights, inputs, cotangent, clip_norm, noise):
    section_index = lax.axis_index("pipe")
    group_count = lax.axis_size("dp")
    weight_block = weights[0]
    local_inputs = inputs[0]
    micro_count, example_count, length_count, width_part = local_inputs.shape
    token_count = example_count * length_count
    column_part = weight_block.shape[1]
    full_width = column_part * group_count
    is_last = section_index == 1

    gathered_inputs = lax.all_gather(local_inputs, "dp", axis=1, tiled=True)
    input_grams = lax.psum(token_grams(local_inputs), "tensor")
    other_input_grams = swapped(input_grams, "pipe")

    own_cotangent = lax.dynamic_index_in_dim(cotangent, section_index, 0, keepdims=False)
    last_grams, last_blocks = column_blocks(own_cotangent, group_count, column_part)
    last_blocks_other = swapped(last_blocks, "pipe")

    last_weights = jnp.where(is_last, weight_block, swapped(weight_block, "pipe"))
    terms = lax.dot_general(
        last_blocks, last_weights, (((1,), (1,)), ((), ())), preferred_element_type=jnp.float32
    ).astype(jnp.bfloat16)
    summed = lax.psum_scatter(terms, "dp", scatter_dimension=0, tiled=True).astype(jnp.float32)
    renewed = (own_cotangent.reshape(token_count, width_part).astype(jnp.float32) + summed).astype(
        jnp.bfloat16
    ).reshape(example_count, length_count, width_part)
    first_grams, first_blocks = column_blocks(renewed, group_count, column_part)
    first_blocks_other = swapped(first_blocks, "pipe")

    own_input_grams = lax.dynamic_index_in_dim(input_grams, section_index, 0, keepdims=False)
    held_input_grams = lax.dynamic_index_in_dim(other_input_grams, section_index, 0, keepdims=False)
    last_input_grams = jnp.where(is_last, own_input_grams, held_input_grams)
    first_input_grams = jnp.where(is_last, held_input_grams, own_input_grams)
    norm_square = jnp.sum(first_input_grams * first_grams, axis=(1, 2)) + jnp.sum(
        last_input_grams * last_grams, axis=(1, 2)
    )
    bound = clip_norm[0]
    own_scales = bound / jnp.maximum(jnp.sqrt(norm_square), bound)
    scale_terms = by_micro(is_last, own_scales, swapped(own_scales, "pipe"))
    scale_pieces, scale_order = ring_pieces(scale_terms, "dp")
    all_scales = jnp.take(scale_pieces, scale_order, axis=0).transpose(1, 0, 2)

    candidates = jnp.stack([first_blocks, first_blocks_other, last_blocks_other, last_blocks])
    grad_blocks = lax.dynamic_slice_in_dim(candidates, micro_count * section_index, micro_count, axis=0)
    scaled_blocks = (
        grad_blocks.reshape(micro_count, group_count, example_count, length_count, column_part).astype(
            jnp.float32
        )
        * all_scales[:, :, :, None, None]
    ).astype(jnp.bfloat16)
    flat_inputs = gathered_inputs.reshape(micro_count * group_count * token_count, width_part)
    flat_grads = scaled_blocks.reshape(micro_count * group_count * token_count, column_part)
    summed_grad = lax.dot_general(
        flat_inputs, flat_grads, (((0,), (0,)), ((), ())), preferred_element_type=jnp.float32
    )
    noise_weight = 1.5 / full_width
    per_example_sum = micro_count * group_count * example_count
    final_output = (
        summed_grad + noise_weight * bound * noise[0].astype(jnp.float32)
    ) / per_example_sum
    return (final_output[None], scale_terms)


def solution(mesh):
    in_specs = (
        P("pipe", "tensor", "dp"),
        P("pipe", None, "dp", None, "tensor"),
        P(None, "dp", None, "tensor"),
        P(),
        P("pipe", "tensor", "dp"),
    )
    out_specs = (P("pipe", "tensor", "dp"), P(None, "dp"))
    return jax.shard_map(local, mesh=mesh, in_specs=in_specs, out_specs=out_specs, check_vma=False)
```
